256 devices in a mesh: dp: 32 (over z, x), tensor: 8 (over y, core).
Axes of the slice: x: 4, y: 4, z: 8, core: 2. Of those that a mesh axis runs over, the one named last changes fastest.
Arguments:
- gradients: float32 [32, 2368, 1024], P('dp', None, 'tensor'), may hold values from -96 to 96
- weights: float32 [2368, 1024], P(None, 'tensor'), may hold values from -64 to 64
- first_moment: float32 [2368, 1024], P(None, 'tensor'), may hold values from -64 to 64
- second_moment: float32 [2368, 1024], P(None, 'tensor'), may hold values from 0.05 to 2
Outputs:
- weights_new: float32 [2368, 1024], P(None, 'tensor')
- first_new: float32 [2368, 1024], P(None, 'tensor')
- second_new: float32 [2368, 1024], P(None, 'tensor')
- copies: bfloat16 [2368, 1024], replicated
- ratios: float32 [4], replicated
The draws below stay inside these ranges and needn't reach their ends.
All inputs are finite; a program needn't handle non-finite values.
Results may differ from the reference program's by a relative error of at most 0.0004.
Values may be sent and summed in bfloat16 or wider, within the bound.
No kernel may reach another device: no remote copies, remote signals or barrier semaphores. Data moves between devices by JAX's collectives and lax.ppermute only.
A program may use at most 64 MiB of HBM per device.

```python
import math
import jax
import jax.numpy as jnp
from jax import lax

D = 1024
HID = 1342
ROWS = 2368
N_DP = 32


def scaled_field(key):
    key_vals, key_cols = jax.random.split(key, 2)
    columns = jnp.arange(D).astype(jnp.float32)
    trend = 1.0 + 2.0 * columns / (D - 1)
    spread = jnp.exp(jax.random.uniform(key_cols, (D,), jnp.float32) * math.log(3.0))
    scale = trend * spread / 3.0
    values = jnp.clip(jax.random.normal(key_vals, (ROWS, D), jnp.float32), -4.0, 4.0)
    scale = scale[None, :]
    return (values * scale).astype(jnp.float32)


def draw_weights(key, part):
    return scaled_field(jax.random.fold_in(key, 11))


def draw_first_moment(key, part):
    return scaled_field(jax.random.fold_in(key, 12))


def steps_of(rng, shape, shards, smallest, high):
    loudness = 1.0
    for dim, shards_of in shards:
        heights = jax.random.uniform(jax.random.fold_in(jax.random.fold_in(rng, 6), dim), (shards_of,), jnp.float32, smallest / len(shards), high / len(shards))
        loudness = loudness * jnp.repeat(jnp.exp(heights), shape[dim] // shards_of).reshape((-1,) + (1,) * (len(shape) - 1 - dim))
    return loudness


def normal_values(rng, shape, scale, limit, cuts=(), held_as=jnp.bfloat16):
    drawn = scale * jax.random.normal(rng, shape, jnp.float32)
    if cuts:
        drawn = drawn * steps_of(rng, shape, cuts, -0.22, 0.18)
    return jnp.clip(drawn, -limit, limit).astype(held_as)


def setup_inputs(seed: int = 0) -> dict:
    key_of = jax.random.split(jax.random.key(seed), 5)
    gradients = normal_values(key_of[0], (N_DP, ROWS, D), 16.0, 96.0, ((0, 32), (2, 8)), jnp.float32)
    weights = draw_weights(jax.random.fold_in(key_of[4], 71), 0)
    first_moment = draw_first_moment(jax.random.fold_in(key_of[4], 71), 0)
    second_moment = jnp.clip(jnp.exp(math.log(2.0) - 3.6888794 * jax.random.uniform(key_of[3], (ROWS, D), jnp.float32) ** steps_of(key_of[3], (ROWS, D), ((1, 8),), -0.2, 0.2)), 0.05, 2.0)
    return {"gradients": gradients, "weights": weights, "first_moment": first_moment, "second_moment": second_moment}


beta_one = 0.9
beta_two = 0.999
correct_one = 1.0 - 0.9 ** 20
correct_two = 1.0 - 0.999 ** 20
epsilon = 1e-06
learn_rate = 0.01
decay_rate = 0.01

def reference(gradients, weights, first_moment, second_moment):
    grad = lax.optimization_barrier(jnp.sum(gradients, axis=0)) / N_DP
    first_new = beta_one * first_moment + (1.0 - beta_one) * grad
    second_new = beta_two * second_moment + (1.0 - beta_two) * grad * grad
    row_ids = jnp.arange(D + HID + 2)
    decay = jnp.where(row_ids < D + HID, decay_rate, 0.0).astype(jnp.float32)
    update = first_new / correct_one / (jnp.sqrt(second_new / correct_two) + epsilon) + decay[:, None] * weights
    bounds = [(0, D), (D, D + HID), (D + HID, D + HID + 1), (D + HID + 1, D + HID + 2)]
    ratio_list = []
    for lower, upper in bounds:
        wsum = jnp.sum(weights[lower:upper] * weights[lower:upper])
        usum = jnp.sum(update[lower:upper] * update[lower:upper])
        ratio_list.append(jnp.sqrt(wsum) / jnp.sqrt(usum))
    ratios = jnp.stack(ratio_list).astype(jnp.float32)
    group = jnp.where(row_ids < D, 0, jnp.where(row_ids < D + HID, 1, row_ids - D - HID + 2))
    row_ratio = ratios[group]
    weights_new = weights - learn_rate * row_ratio[:, None] * update
    copies = weights_new.astype(jnp.bfloat16)
    return (weights_new, first_new, second_new, copies, ratios)
```

```python
import jax
import jax.numpy as jnp
import numpy as np
from jax import lax
from jax.sharding import Mesh
from jax.sharding import PartitionSpec as P

D = 1024
HID = 1342


beta_one = 0.9
beta_two = 0.999
correct_one = 1.0 - 0.9**20
correct_two = 1.0 - 0.999**20
epsilon = 1e-06
learn_rate = 0.01
decay_rate = 0.01

DP = ("z", "x")
TN = ("y", "core")


def group_table(row_count):
    row_ids = lax.broadcasted_iota(jnp.int32, (row_count, 4), 0)
    which = lax.broadcasted_iota(jnp.int32, (row_count, 4), 1)
    group = jnp.where(row_ids < D, 0, jnp.where(row_ids < D + HID, 1, row_ids - D - HID + 2))
    return (group == which).astype(jnp.float32)


def group_squares(values, seg_table):
    row_sums = jnp.sum(values * values, axis=1)
    return jnp.dot(row_sums, seg_table, precision=lax.Precision.HIGHEST)


def adam_part(grad, weights, first_moment, second_moment, seg_table):
    first_new = beta_one * first_moment + (1.0 - beta_one) * grad
    second_new = beta_two * second_moment + (1.0 - beta_two) * grad * grad
    decay = decay_rate * (seg_table[:, 0] + seg_table[:, 1])
    update = (
        first_new / correct_one / (jnp.sqrt(second_new / correct_two) + epsilon)
        + decay[:, None] * weights
    )
    return (first_new, second_new, update)


def apply_ratios(weights, update, seg_table, weight_total, step_total):
    ratios = jnp.sqrt(weight_total) / jnp.sqrt(step_total)
    row_ratio = jnp.dot(seg_table, ratios, precision=lax.Precision.HIGHEST)
    return (weights - learn_rate * row_ratio[:, None] * update, ratios)


def dp_sum(x, nz, nx):
    rows, cols = x.shape
    unit = 8 * nz * nx
    padded = -(-rows // unit) * unit
    y = jnp.pad(x, ((0, padded - rows), (0, 0)))
    y = lax.all_to_all(y.reshape(nx, padded // nx, cols), "x", 0, 0, tiled=False).sum(0)
    y = lax.all_to_all(y.reshape(nz, padded // (nx * nz), cols), "z", 0, 0, tiled=False).sum(0)
    y = lax.all_to_all(jnp.broadcast_to(y[None], (nz,) + y.shape), "z", 0, 0, tiled=False)
    y = y.reshape(padded // nx, cols)
    y = lax.all_to_all(jnp.broadcast_to(y[None], (nx,) + y.shape), "x", 0, 0, tiled=False)
    return y.reshape(padded, cols)[:rows]


def tensor_sum(v, ny, ncore):
    for axis, size in (("core", ncore), ("y", ny)):
        step = 1
        while step < size:
            v = v + lax.ppermute(v, axis, [(i, i ^ step) for i in range(size)])
            step *= 2
    return v


def make_shards(nz, nx, ny, ncore):
    def shards(gradients, weights, first_moment, second_moment):
        local_grad = gradients[0]
        row_count = weights.shape[0]
        seg_table = group_table(row_count)
        grad = dp_sum(local_grad, nz, nx) / (nz * nx)
        first_new, second_new, update = adam_part(grad, weights, first_moment, second_moment, seg_table)
        both = jnp.concatenate([group_squares(weights, seg_table), group_squares(update, seg_table)])
        both = tensor_sum(both, ny, ncore)
        weight_total, step_total = both[:4], both[4:]
        weights_new, ratios = apply_ratios(weights, update, seg_table, weight_total, step_total)
        copies = lax.all_gather(weights_new.astype(jnp.bfloat16), TN, axis=1, tiled=True)
        return (weights_new, first_new, second_new, copies, ratios)

    return shards


def physical_mesh(mesh):
    devices = mesh.devices
    dp_devices = devices[:, 0]
    nx = len({d.coords[0] for d in dp_devices})
    nz = dp_devices.size // nx
    tn_devices = devices[0, :]
    ncore = len({d.core_on_chip for d in tn_devices})
    ny = tn_devices.size // ncore
    return Mesh(devices.reshape(nz, nx, ny, ncore), ("z", "x", "y", "core")), (nz, nx, ny, ncore)


def solution(mesh):
    mesh2, sizes = physical_mesh(mesh)
    return jax.shard_map(
        make_shards(*sizes),
        mesh=mesh2,
        in_specs=(P(DP, None, TN), P(None, TN), P(None, TN), P(None, TN)),
        out_specs=(P(None, TN), P(None, TN), P(None, TN), P(), P()),
        check_vma=False,
    )
```

```python
import jax
import jax.numpy as jnp
import numpy as np
from jax import lax
from jax.sharding import Mesh
from jax.sharding import PartitionSpec as P

D = 1024
HID = 1342


beta_one = 0.9
beta_two = 0.999
correct_one = 1.0 - 0.9**20
correct_two = 1.0 - 0.999**20
epsilon = 1e-06
learn_rate = 0.01
decay_rate = 0.01

DP = ("z", "x")
TN = ("y", "core")


def group_table(row_count):
    row_ids = lax.broadcasted_iota(jnp.int32, (row_count, 4), 0)
    which = lax.broadcasted_iota(jnp.int32, (row_count, 4), 1)
    group = jnp.where(row_ids < D, 0, jnp.where(row_ids < D + HID, 1, row_ids - D - HID + 2))
    return (group == which).astype(jnp.float32)


def group_squares(values, seg_table):
    row_sums = jnp.sum(values * values, axis=1)
    return jnp.dot(row_sums, seg_table, precision=lax.Precision.HIGHEST)


def adam_part(grad, weights, first_moment, second_moment, seg_table):
    first_new = beta_one * first_moment + (1.0 - beta_one) * grad
    second_new = beta_two * second_moment + (1.0 - beta_two) * grad * grad
    decay = decay_rate * (seg_table[:, 0] + seg_table[:, 1])
    update = (
        first_new / correct_one / (jnp.sqrt(second_new / correct_two) + epsilon)
        + decay[:, None] * weights
    )
    return (first_new, second_new, update)


def apply_ratios(weights, update, seg_table, weight_total, step_total):
    ratios = jnp.sqrt(weight_total) / jnp.sqrt(step_total)
    row_ratio = jnp.dot(seg_table, ratios, precision=lax.Precision.HIGHEST)
    return (weights - learn_rate * row_ratio[:, None] * update, ratios)


def dp_sum(x, nz, nx):
    rows, cols = x.shape
    unit = 8 * nz * nx
    padded = -(-rows // unit) * unit
    y = jnp.pad(x, ((0, padded - rows), (0, 0)))
    y = lax.all_to_all(y.reshape(nx, padded // nx, cols), "x", 0, 0, tiled=False).sum(0)
    y = lax.all_to_all(y.reshape(nz, padded // (nx * nz), cols), "z", 0, 0, tiled=False).sum(0)
    y = lax.all_to_all(jnp.broadcast_to(y[None], (nz,) + y.shape), "z", 0, 0, tiled=False)
    y = y.reshape(padded // nx, cols)
    y = lax.all_to_all(jnp.broadcast_to(y[None], (nx,) + y.shape), "x", 0, 0, tiled=False)
    return y.reshape(padded, cols)[:rows]


def tensor_sum(v, ny, ncore):
    for axis, size in (("core", ncore), ("y", ny)):
        step = 1
        while step < size:
            v = v + lax.ppermute(v, axis, [(i, i ^ step) for i in range(size)])
            step *= 2
    return v


def tensor_gather(b, ny):
    y = lax.axis_index("y")
    core = lax.axis_index("core")
    swap = [(0, 1), (1, 0)]
    mine = [b] + [lax.ppermute(b, "y", [(i, (i - s) % ny) for i in range(ny)]) for s in range(1, ny)]
    other = [lax.ppermute(m, "core", swap) for m in mine]
    pairs = [
        jnp.where(core == 0, jnp.concatenate([m, o], 1), jnp.concatenate([o, m], 1))
        for m, o in zip(mine, other)
    ]
    q = jnp.concatenate(pairs + pairs, 1)
    width = 2 * b.shape[1]
    return lax.dynamic_slice_in_dim(q, ((ny - y) % ny) * width, ny * width, 1)


def make_shards(nz, nx, ny, ncore):
    def shards(gradients, weights, first_moment, second_moment):
        local_grad = gradients[0]
        row_count = weights.shape[0]
        seg_table = group_table(row_count)
        grad = dp_sum(local_grad, nz, nx) / (nz * nx)
        first_new, second_new, update = adam_part(grad, weights, first_moment, second_moment, seg_table)
        both = jnp.concatenate([group_squares(weights, seg_table), group_squares(update, seg_table)])
        both = tensor_sum(both, ny, ncore)
        weight_total, step_total = both[:4], both[4:]
        weights_new, ratios = apply_ratios(weights, update, seg_table, weight_total, step_total)
        if ncore == 2:
            copies = tensor_gather(weights_new.astype(jnp.bfloat16), ny)
        else:
            copies = lax.all_gather(weights_new.astype(jnp.bfloat16), TN, axis=1, tiled=True)
        return (weights_new, first_new, second_new, copies, ratios)

    return shards


def physical_mesh(mesh):
    devices = mesh.devices
    dp_devices = devices[:, 0]
    nx = len({d.coords[0] for d in dp_devices})
    nz = dp_devices.size // nx
    tn_devices = devices[0, :]
    ncore = len({d.core_on_chip for d in tn_devices})
    ny = tn_devices.size // ncore
    return Mesh(devices.reshape(nz, nx, ny, ncore), ("z", "x", "y", "core")), (nz, nx, ny, ncore)


def solution(mesh):
    mesh2, sizes = physical_mesh(mesh)
    return jax.shard_map(
        make_shards(*sizes),
        mesh=mesh2,
        in_specs=(P(DP, None, TN), P(None, TN), P(None, TN), P(None, TN)),
        out_specs=(P(None, TN), P(None, TN), P(None, TN), P(), P()),
        check_vma=False,
    )
```

```python
import jax
import jax.numpy as jnp
import numpy as np
from jax import lax
from jax.sharding import Mesh
from jax.sharding import PartitionSpec as P

D = 1024
HID = 1342


beta_one = 0.9
beta_two = 0.999
correct_one = 1.0 - 0.9**20
correct_two = 1.0 - 0.999**20
epsilon = 1e-06
learn_rate = 0.01
decay_rate = 0.01

DP = ("z", "x")
TN = ("y", "core")


def group_table(row_count):
    row_ids = lax.broadcasted_iota(jnp.int32, (row_count, 4), 0)
    which = lax.broadcasted_iota(jnp.int32, (row_count, 4), 1)
    group = jnp.where(row_ids < D, 0, jnp.where(row_ids < D + HID, 1, row_ids - D - HID + 2))
    return (group == which).astype(jnp.float32)


def group_squares(values, seg_table):
    row_sums = jnp.sum(values * values, axis=1)
    return jnp.dot(row_sums, seg_table, precision=lax.Precision.HIGHEST)


def adam_part(grad, weights, first_moment, second_moment, seg_table):
    first_new = beta_one * first_moment + (1.0 - beta_one) * grad
    second_new = beta_two * second_moment + (1.0 - beta_two) * grad * grad
    decay = decay_rate * (seg_table[:, 0] + seg_table[:, 1])
    update = (
        first_new / correct_one / (jnp.sqrt(second_new / correct_two) + epsilon)
        + decay[:, None] * weights
    )
    return (first_new, second_new, update)


def apply_ratios(weights, update, seg_table, weight_total, step_total):
    ratios = jnp.sqrt(weight_total) / jnp.sqrt(step_total)
    row_ratio = jnp.dot(seg_table, ratios, precision=lax.Precision.HIGHEST)
    return (weights - learn_rate * row_ratio[:, None] * update, ratios)


def dp_sum(x, nz, nx):
    rows, cols = x.shape
    part = rows // nx
    padded = -(-part // (8 * nz)) * (8 * nz)
    y = lax.all_to_all(x.reshape(nx, part, cols), "x", 0, 0, tiled=False).sum(0)
    y = jnp.pad(y, ((0, padded - part), (0, 0)))
    y = lax.all_to_all(y.reshape(nz, padded // nz, cols), "z", 0, 0, tiled=False).sum(0)
    y = lax.all_to_all(jnp.broadcast_to(y[None], (nz,) + y.shape), "z", 0, 0, tiled=False)
    y = y.reshape(padded, cols)[:part]
    y = lax.all_to_all(jnp.broadcast_to(y[None], (nx,) + y.shape), "x", 0, 0, tiled=False)
    return y.reshape(rows, cols)


def tensor_sum(v, ny, ncore):
    if ncore == 2:
        v = v + lax.ppermute(v, "core", [(0, 1), (1, 0)])
    else:
        v = lax.psum(v, "core")
    y = lax.axis_index("y")
    slots = jnp.zeros((ny,) + v.shape, v.dtype)
    slots = lax.dynamic_update_index_in_dim(slots, v, y, 0)
    for s in range(1, ny):
        got = lax.ppermute(v, "y", [(i, (i - s) % ny) for i in range(ny)])
        slots = lax.dynamic_update_index_in_dim(slots, got, (y + s) % ny, 0)
    total = slots[0]
    for k in range(1, ny):
        total = total + slots[k]
    return total


def tensor_gather(b, ny):
    y = lax.axis_index("y")
    core = lax.axis_index("core")
    swap = [(0, 1), (1, 0)]
    mine = [b] + [lax.ppermute(b, "y", [(i, (i - s) % ny) for i in range(ny)]) for s in range(1, ny)]
    other = [lax.ppermute(m, "core", swap) for m in mine]
    pairs = [
        jnp.where(core == 0, jnp.concatenate([m, o], 1), jnp.concatenate([o, m], 1))
        for m, o in zip(mine, other)
    ]
    q = jnp.concatenate(pairs + pairs, 1)
    width = 2 * b.shape[1]
    return lax.dynamic_slice_in_dim(q, ((ny - y) % ny) * width, ny * width, 1)


def make_shards(nz, nx, ny, ncore):
    def shards(gradients, weights, first_moment, second_moment):
        local_grad = gradients[0]
        row_count = weights.shape[0]
        seg_table = group_table(row_count)
        grad = dp_sum(local_grad, nz, nx) / (nz * nx)
        first_new, second_new, update = adam_part(grad, weights, first_moment, second_moment, seg_table)
        both = jnp.concatenate([group_squares(weights, seg_table), group_squares(update, seg_table)])
        both = tensor_sum(both, ny, ncore)
        weight_total, step_total = both[:4], both[4:]
        weights_new, ratios = apply_ratios(weights, update, seg_table, weight_total, step_total)
        if ncore == 2:
            copies = tensor_gather(weights_new.astype(jnp.bfloat16), ny)
        else:
            copies = lax.all_gather(weights_new.astype(jnp.bfloat16), TN, axis=1, tiled=True)
        return (weights_new, first_new, second_new, copies, ratios)

    return shards


def physical_mesh(mesh):
    devices = mesh.devices
    dp_devices = devices[:, 0]
    nx = len({d.coords[0] for d in dp_devices})
    nz = dp_devices.size // nx
    tn_devices = devices[0, :]
    ncore = len({d.core_on_chip for d in tn_devices})
    ny = tn_devices.size // ncore
    return Mesh(devices.reshape(nz, nx, ny, ncore), ("z", "x", "y", "core")), (nz, nx, ny, ncore)


def solution(mesh):
    mesh2, sizes = physical_mesh(mesh)
    return jax.shard_map(
        make_shards(*sizes),
        mesh=mesh2,
        in_specs=(P(DP, None, TN), P(None, TN), P(None, TN), P(None, TN)),
        out_specs=(P(None, TN), P(None, TN), P(None, TN), P(), P()),
        check_vma=False,
    )
```

```python
import jax
import jax.numpy as jnp
import numpy as np
from jax import lax
from jax.sharding import Mesh
from jax.sharding import PartitionSpec as P

D = 1024
HID = 1342


beta_one = 0.9
beta_two = 0.999
correct_one = 1.0 - 0.9**20
correct_two = 1.0 - 0.999**20
epsilon = 1e-06
learn_rate = 0.01
decay_rate = 0.01

DP = ("z", "x")
TN = ("y", "core")


def group_table(row_count):
    row_ids = lax.broadcasted_iota(jnp.int32, (row_count, 4), 0)
    which = lax.broadcasted_iota(jnp.int32, (row_count, 4), 1)
    group = jnp.where(row_ids < D, 0, jnp.where(row_ids < D + HID, 1, row_ids - D - HID + 2))
    return (group == which).astype(jnp.float32)


def group_squares(values, seg_table):
    row_sums = jnp.sum(values * values, axis=1)
    return jnp.dot(row_sums, seg_table, precision=lax.Precision.HIGHEST)


def adam_part(grad, weights, first_moment, second_moment, seg_table):
    first_new = beta_one * first_moment + (1.0 - beta_one) * grad
    second_new = beta_two * second_moment + (1.0 - beta_two) * grad * grad
    decay = decay_rate * (seg_table[:, 0] + seg_table[:, 1])
    update = (
        first_new / correct_one / (jnp.sqrt(second_new / correct_two) + epsilon)
        + decay[:, None] * weights
    )
    return (first_new, second_new, update)


def apply_ratios(weights, update, seg_table, weight_total, step_total):
    ratios = jnp.sqrt(weight_total) / jnp.sqrt(step_total)
    row_ratio = jnp.dot(seg_table, ratios, precision=lax.Precision.HIGHEST)
    return (weights - learn_rate * row_ratio[:, None] * update, ratios)


def dp_sum(x, nz, nx):
    rows, cols = x.shape
    part = rows // nx
    padded = -(-part // (8 * nz)) * (8 * nz)
    y = lax.all_to_all(x.reshape(nx, part, cols), "x", 0, 0, tiled=False).sum(0)
    y = jnp.pad(y, ((0, padded - part), (0, 0)))
    y = lax.all_to_all(y.reshape(nz, padded // nz, cols), "z", 0, 0, tiled=False).sum(0)
    y = lax.all_to_all(jnp.broadcast_to(y[None], (nz,) + y.shape), "z", 0, 0, tiled=False)
    y = y.reshape(padded, cols)[:part]
    y = lax.all_to_all(jnp.broadcast_to(y[None], (nx,) + y.shape), "x", 0, 0, tiled=False)
    return y.reshape(rows, cols)


def tensor_sum(v, ny, ncore):
    if ncore == 2:
        v = v + lax.ppermute(v, "core", [(0, 1), (1, 0)])
    else:
        v = lax.psum(v, "core")
    y = lax.axis_index("y")
    slots = jnp.zeros((ny,) + v.shape, v.dtype)
    slots = lax.dynamic_update_index_in_dim(slots, v, y, 0)
    for s in range(1, ny):
        got = lax.ppermute(v, "y", [(i, (i - s) % ny) for i in range(ny)])
        slots = lax.dynamic_update_index_in_dim(slots, got, (y + s) % ny, 0)
    total = slots[0]
    for k in range(1, ny):
        total = total + slots[k]
    return total


def tensor_gather(b, ny):
    y = lax.axis_index("y")
    core = lax.axis_index("core")
    swap = [(0, 1), (1, 0)]
    width = b.shape[1]
    out = jnp.zeros((b.shape[0], 2 * ny * width), b.dtype)
    for s in range(ny):
        mine = b if s == 0 else lax.ppermute(b, "y", [(i, (i - s) % ny) for i in range(ny)])
        other = lax.ppermute(mine, "core", swap)
        chip = (y + s) % ny
        out = lax.dynamic_update_slice_in_dim(out, mine, (2 * chip + core) * width, 1)
        out = lax.dynamic_update_slice_in_dim(out, other, (2 * chip + 1 - core) * width, 1)
    return out


def make_shards(nz, nx, ny, ncore):
    def shards(gradients, weights, first_moment, second_moment):
        local_grad = gradients[0]
        row_count = weights.shape[0]
        seg_table = group_table(row_count)
        grad = dp_sum(local_grad, nz, nx) / (nz * nx)
        first_new, second_new, update = adam_part(grad, weights, first_moment, second_moment, seg_table)
        both = jnp.concatenate([group_squares(weights, seg_table), group_squares(update, seg_table)])
        both = tensor_sum(both, ny, ncore)
        weight_total, step_total = both[:4], both[4:]
        weights_new, ratios = apply_ratios(weights, update, seg_table, weight_total, step_total)
        if ncore == 2:
            copies = tensor_gather(weights_new.astype(jnp.bfloat16), ny)
        else:
            copies = lax.all_gather(weights_new.astype(jnp.bfloat16), TN, axis=1, tiled=True)
        return (weights_new, first_new, second_new, copies, ratios)

    return shards


def physical_mesh(mesh):
    devices = mesh.devices
    dp_devices = devices[:, 0]
    nx = len({d.coords[0] for d in dp_devices})
    nz = dp_devices.size // nx
    tn_devices = devices[0, :]
    ncore = len({d.core_on_chip for d in tn_devices})
    ny = tn_devices.size // ncore
    return Mesh(devices.reshape(nz, nx, ny, ncore), ("z", "x", "y", "core")), (nz, nx, ny, ncore)


def solution(mesh):
    mesh2, sizes = physical_mesh(mesh)
    return jax.shard_map(
        make_shards(*sizes),
        mesh=mesh2,
        in_specs=(P(DP, None, TN), P(None, TN), P(None, TN), P(None, TN)),
        out_specs=(P(None, TN), P(None, TN), P(None, TN), P(), P()),
        check_vma=False,
    )
```

```python
import jax
import jax.numpy as jnp
import numpy as np
from jax import lax
from jax.sharding import Mesh
from jax.sharding import PartitionSpec as P

D = 1024
HID = 1342


beta_one = 0.9
beta_two = 0.999
correct_one = 1.0 - 0.9**20
correct_two = 1.0 - 0.999**20
epsilon = 1e-06
learn_rate = 0.01
decay_rate = 0.01

DP = ("z", "x")
TN = ("y", "core")


def group_table(row_count):
    row_ids = lax.broadcasted_iota(jnp.int32, (row_count, 4), 0)
    which = lax.broadcasted_iota(jnp.int32, (row_count, 4), 1)
    group = jnp.where(row_ids < D, 0, jnp.where(row_ids < D + HID, 1, row_ids - D - HID + 2))
    return (group == which).astype(jnp.float32)


def group_squares(values, seg_table):
    row_sums = jnp.sum(values * values, axis=1)
    return jnp.dot(row_sums, seg_table, precision=lax.Precision.HIGHEST)


def adam_part(grad, weights, first_moment, second_moment, seg_table):
    first_new = beta_one * first_moment + (1.0 - beta_one) * grad
    second_new = beta_two * second_moment + (1.0 - beta_two) * grad * grad
    decay = decay_rate * (seg_table[:, 0] + seg_table[:, 1])
    update = (
        first_new / correct_one / (jnp.sqrt(second_new / correct_two) + epsilon)
        + decay[:, None] * weights
    )
    return (first_new, second_new, update)


def apply_ratios(weights, update, seg_table, weight_total, step_total):
    ratios = jnp.sqrt(weight_total) / jnp.sqrt(step_total)
    row_ratio = jnp.dot(seg_table, ratios, precision=lax.Precision.HIGHEST)
    return (weights - learn_rate * row_ratio[:, None] * update, ratios)


def dp_sum(x, nz, nx):
    rows, cols = x.shape
    part = rows // nx
    padded = -(-part // (8 * nz)) * (8 * nz)
    y = lax.all_to_all(x.reshape(nx, part, cols), "x", 0, 0, tiled=False).sum(0)
    y = jnp.pad(y, ((0, padded - part), (0, 0)))
    y = lax.all_to_all(y.reshape(nz, padded // nz, cols), "z", 0, 0, tiled=False).sum(0)
    y = lax.all_to_all(jnp.broadcast_to(y[None], (nz,) + y.shape), "z", 0, 0, tiled=False)
    y = y.reshape(padded, cols)[:part]
    y = lax.all_to_all(jnp.broadcast_to(y[None], (nx,) + y.shape), "x", 0, 0, tiled=False)
    return y.reshape(rows, cols)


def tensor_sum(v, ny, ncore):
    if ncore == 2:
        v = v + lax.ppermute(v, "core", [(0, 1), (1, 0)])
    else:
        v = lax.psum(v, "core")
    y = lax.axis_index("y")
    slots = jnp.zeros((ny,) + v.shape, v.dtype)
    slots = lax.dynamic_update_index_in_dim(slots, v, y, 0)
    for s in range(1, ny):
        got = lax.ppermute(v, "y", [(i, (i - s) % ny) for i in range(ny)])
        slots = lax.dynamic_update_index_in_dim(slots, got, (y + s) % ny, 0)
    total = slots[0]
    for k in range(1, ny):
        total = total + slots[k]
    return total


def tensor_gather(b, ny):
    y = lax.axis_index("y")
    core = lax.axis_index("core")
    swap = [(0, 1), (1, 0)]
    rows, width = b.shape

    def shift(v, s):
        return lax.ppermute(v, "y", [(i, (i - s) % ny) for i in range(ny)])

    if ny == 4 and rows % 16 == 0:
        half = rows // 2
        plus, minus = shift(b, 1), shift(b, -1)
        pieces = [(b, 0, 0), (plus, 1, 0), (minus, 3, 0), (shift(plus[:half], 1), 2, 0), (shift(minus[half:], -1), 2, half)]
    else:
        pieces = [(b, 0, 0)] + [(shift(b, s), s, 0) for s in range(1, ny)]
    out = jnp.zeros((rows, 2 * ny * width), b.dtype)
    for mine, s, row in pieces:
        other = lax.ppermute(mine, "core", swap)
        chip = (y + s) % ny
        out = lax.dynamic_update_slice(out, mine, (row, (2 * chip + core) * width))
        out = lax.dynamic_update_slice(out, other, (row, (2 * chip + 1 - core) * width))
    return out


def make_shards(nz, nx, ny, ncore):
    def shards(gradients, weights, first_moment, second_moment):
        local_grad = gradients[0]
        row_count = weights.shape[0]
        seg_table = group_table(row_count)
        grad = dp_sum(local_grad, nz, nx) / (nz * nx)
        first_new, second_new, update = adam_part(grad, weights, first_moment, second_moment, seg_table)
        both = jnp.concatenate([group_squares(weights, seg_table), group_squares(update, seg_table)])
        both = tensor_sum(both, ny, ncore)
        weight_total, step_total = both[:4], both[4:]
        weights_new, ratios = apply_ratios(weights, update, seg_table, weight_total, step_total)
        if ncore == 2:
            copies = tensor_gather(weights_new.astype(jnp.bfloat16), ny)
        else:
            copies = lax.all_gather(weights_new.astype(jnp.bfloat16), TN, axis=1, tiled=True)
        return (weights_new, first_new, second_new, copies, ratios)

    return shards


def physical_mesh(mesh):
    devices = mesh.devices
    dp_devices = devices[:, 0]
    nx = len({d.coords[0] for d in dp_devices})
    nz = dp_devices.size // nx
    tn_devices = devices[0, :]
    ncore = len({d.core_on_chip for d in tn_devices})
    ny = tn_devices.size // ncore
    return Mesh(devices.reshape(nz, nx, ny, ncore), ("z", "x", "y", "core")), (nz, nx, ny, ncore)


def solution(mesh):
    mesh2, sizes = physical_mesh(mesh)
    return jax.shard_map(
        make_shards(*sizes),
        mesh=mesh2,
        in_specs=(P(DP, None, TN), P(None, TN), P(None, TN), P(None, TN)),
        out_specs=(P(None, TN), P(None, TN), P(None, TN), P(), P()),
        check_vma=False,
    )
```

```python
import jax
import jax.numpy as jnp
import numpy as np
from jax import lax
from jax.sharding import Mesh
from jax.sharding import PartitionSpec as P

D = 1024
HID = 1342


beta_one = 0.9
beta_two = 0.999
correct_one = 1.0 - 0.9**20
correct_two = 1.0 - 0.999**20
epsilon = 1e-06
learn_rate = 0.01
decay_rate = 0.01

DP = ("z", "x")
TN = ("y", "core")


def group_table(row_count):
    row_ids = lax.broadcasted_iota(jnp.int32, (row_count, 4), 0)
    which = lax.broadcasted_iota(jnp.int32, (row_count, 4), 1)
    group = jnp.where(row_ids < D, 0, jnp.where(row_ids < D + HID, 1, row_ids - D - HID + 2))
    return (group == which).astype(jnp.float32)


def group_squares(values, seg_table):
    row_sums = jnp.sum(values * values, axis=1)
    return jnp.dot(row_sums, seg_table, precision=lax.Precision.HIGHEST)


def adam_part(grad, weights, first_moment, second_moment, seg_table):
    first_new = beta_one * first_moment + (1.0 - beta_one) * grad
    second_new = beta_two * second_moment + (1.0 - beta_two) * grad * grad
    decay = decay_rate * (seg_table[:, 0] + seg_table[:, 1])
    update = (
        first_new / correct_one / (jnp.sqrt(second_new / correct_two) + epsilon)
        + decay[:, None] * weights
    )
    return (first_new, second_new, update)


def apply_ratios(weights, update, seg_table, weight_total, step_total):
    ratios = jnp.sqrt(weight_total) / jnp.sqrt(step_total)
    row_ratio = jnp.dot(seg_table, ratios, precision=lax.Precision.HIGHEST)
    return (weights - learn_rate * row_ratio[:, None] * update, ratios)


def dp_sum(x, nz, nx):
    rows, cols = x.shape
    part = rows // nx
    padded = -(-part // (8 * nz)) * (8 * nz)
    y = lax.all_to_all(x.reshape(nx, part, cols), "x", 0, 0, tiled=False).sum(0)
    y = jnp.pad(y, ((0, padded - part), (0, 0)))
    y = lax.all_to_all(y.reshape(nz, padded // nz, cols), "z", 0, 0, tiled=False).sum(0)
    y = lax.all_to_all(jnp.broadcast_to(y[None], (nz,) + y.shape), "z", 0, 0, tiled=False)
    y = y.reshape(padded, cols)[:part]
    y = lax.all_to_all(jnp.broadcast_to(y[None], (nx,) + y.shape), "x", 0, 0, tiled=False)
    return y.reshape(rows, cols)


def tensor_sum(v, ny, ncore):
    if ncore == 2:
        v = v + lax.ppermute(v, "core", [(0, 1), (1, 0)])
    else:
        v = lax.psum(v, "core")
    y = lax.axis_index("y")
    slots = jnp.zeros((ny,) + v.shape, v.dtype)
    slots = lax.dynamic_update_index_in_dim(slots, v, y, 0)
    for s in range(1, ny):
        got = lax.ppermute(v, "y", [(i, (i - s) % ny) for i in range(ny)])
        slots = lax.dynamic_update_index_in_dim(slots, got, (y + s) % ny, 0)
    total = slots[0]
    for k in range(1, ny):
        total = total + slots[k]
    return total


def tensor_gather(b, ny):
    y = lax.axis_index("y")
    core = lax.axis_index("core")
    swap = [(0, 1), (1, 0)]
    rows, width = b.shape

    def shift(v, s):
        return lax.ppermute(v, "y", [(i, (i - s) % ny) for i in range(ny)])

    if ny == 4 and rows % 16 == 0:
        half = rows // 2
        plus, minus = shift(b, 1), shift(b, -1)
        pieces = [(b, 0, 0), (plus, 1, 0), (minus, 3, 0), (shift(plus[:half], 1), 2, 0), (shift(minus[half:], -1), 2, half)]
    else:
        pieces = [(b, 0, 0)] + [(shift(b, s), s, 0) for s in range(1, ny)]
    mines = [m for m, _, _ in pieces]
    others = [lax.ppermute(m, "core", swap) for m in mines]

    def layout(k, c):
        def build(mines, others):
            blocks = []
            for chip in range(ny):
                s = (chip - k) % ny
                parts = [i for i, (_, si, _) in enumerate(pieces) if si == s]
                mine = jnp.concatenate([mines[i] for i in parts], 0)
                other = jnp.concatenate([others[i] for i in parts], 0)
                blocks += [mine, other] if c == 0 else [other, mine]
            return jnp.concatenate(blocks, 1)

        return build

    branches = [layout(k, c) for k in range(ny) for c in range(2)]
    return lax.switch(y * 2 + core, branches, mines, others)


def make_shards(nz, nx, ny, ncore):
    def shards(gradients, weights, first_moment, second_moment):
        local_grad = gradients[0]
        row_count = weights.shape[0]
        seg_table = group_table(row_count)
        grad = dp_sum(local_grad, nz, nx) / (nz * nx)
        first_new, second_new, update = adam_part(grad, weights, first_moment, second_moment, seg_table)
        both = jnp.concatenate([group_squares(weights, seg_table), group_squares(update, seg_table)])
        both = tensor_sum(both, ny, ncore)
        weight_total, step_total = both[:4], both[4:]
        weights_new, ratios = apply_ratios(weights, update, seg_table, weight_total, step_total)
        if ncore == 2:
            copies = tensor_gather(weights_new.astype(jnp.bfloat16), ny)
        else:
            copies = lax.all_gather(weights_new.astype(jnp.bfloat16), TN, axis=1, tiled=True)
        return (weights_new, first_new, second_new, copies, ratios)

    return shards


def physical_mesh(mesh):
    devices = mesh.devices
    dp_devices = devices[:, 0]
    nx = len({d.coords[0] for d in dp_devices})
    nz = dp_devices.size // nx
    tn_devices = devices[0, :]
    ncore = len({d.core_on_chip for d in tn_devices})
    ny = tn_devices.size // ncore
    return Mesh(devices.reshape(nz, nx, ny, ncore), ("z", "x", "y", "core")), (nz, nx, ny, ncore)


def solution(mesh):
    mesh2, sizes = physical_mesh(mesh)
    return jax.shard_map(
        make_shards(*sizes),
        mesh=mesh2,
        in_specs=(P(DP, None, TN), P(None, TN), P(None, TN), P(None, TN)),
        out_specs=(P(None, TN), P(None, TN), P(None, TN), P(), P()),
        check_vma=False,
    )
```

```python
import jax
import jax.numpy as jnp
import numpy as np
from jax import lax
from jax.sharding import Mesh
from jax.sharding import PartitionSpec as P

D = 1024
HID = 1342


beta_one = 0.9
beta_two = 0.999
correct_one = 1.0 - 0.9**20
correct_two = 1.0 - 0.999**20
epsilon = 1e-06
learn_rate = 0.01
decay_rate = 0.01

DP = ("z", "x")
TN = ("y", "core")


def group_table(row_count):
    row_ids = lax.broadcasted_iota(jnp.int32, (row_count, 4), 0)
    which = lax.broadcasted_iota(jnp.int32, (row_count, 4), 1)
    group = jnp.where(row_ids < D, 0, jnp.where(row_ids < D + HID, 1, row_ids - D - HID + 2))
    return (group == which).astype(jnp.float32)


def group_squares(values, seg_table):
    row_sums = jnp.sum(values * values, axis=1)
    return jnp.dot(row_sums, seg_table, precision=lax.Precision.HIGHEST)


def adam_part(grad, weights, first_moment, second_moment, seg_table):
    first_new = beta_one * first_moment + (1.0 - beta_one) * grad
    second_new = beta_two * second_moment + (1.0 - beta_two) * grad * grad
    decay = decay_rate * (seg_table[:, 0] + seg_table[:, 1])
    update = (
        first_new / correct_one / (jnp.sqrt(second_new / correct_two) + epsilon)
        + decay[:, None] * weights
    )
    return (first_new, second_new, update)


def apply_ratios(weights, update, seg_table, weight_total, step_total):
    ratios = jnp.sqrt(weight_total) / jnp.sqrt(step_total)
    row_ratio = jnp.dot(seg_table, ratios, precision=lax.Precision.HIGHEST)
    return (weights - learn_rate * row_ratio[:, None] * update, ratios)


def dp_sum(x, nz, nx):
    rows, cols = x.shape
    part = rows // nx
    padded = -(-part // (8 * nz)) * (8 * nz)
    y = lax.all_to_all(x.reshape(nx, part, cols), "x", 0, 0, tiled=False).sum(0)
    y = jnp.pad(y, ((0, padded - part), (0, 0)))
    y = lax.all_to_all(y.reshape(nz, padded // nz, cols), "z", 0, 0, tiled=False).sum(0)
    y = lax.all_to_all(jnp.broadcast_to(y[None], (nz,) + y.shape), "z", 0, 0, tiled=False)
    own = y.reshape(padded, cols)[:part]
    y = lax.all_to_all(jnp.broadcast_to(own[None], (nx,) + own.shape), "x", 0, 0, tiled=False)
    return y.reshape(rows, cols), own


def axis_sum(v, axis, n):
    me = lax.axis_index(axis)
    slots = jnp.zeros((n,) + v.shape, v.dtype)
    slots = lax.dynamic_update_index_in_dim(slots, v, me, 0)
    for s in range(1, n):
        got = lax.ppermute(v, axis, [(i, (i - s) % n) for i in range(n)])
        slots = lax.dynamic_update_index_in_dim(slots, got, (me + s) % n, 0)
    total = slots[0]
    for k in range(1, n):
        total = total + slots[k]
    return total


def tensor_sum(v, ny, ncore):
    if ncore == 2:
        v = v + lax.ppermute(v, "core", [(0, 1), (1, 0)])
    else:
        v = lax.psum(v, "core")
    return axis_sum(v, "y", ny)


def tensor_gather(b, ny):
    y = lax.axis_index("y")
    core = lax.axis_index("core")
    swap = [(0, 1), (1, 0)]
    rows, width = b.shape

    def shift(v, s):
        return lax.ppermute(v, "y", [(i, (i - s) % ny) for i in range(ny)])

    if ny == 4 and rows % 16 == 0:
        half = rows // 2
        plus, minus = shift(b, 1), shift(b, -1)
        pieces = [(b, 0, 0), (plus, 1, 0), (minus, 3, 0), (shift(plus[:half], 1), 2, 0), (shift(minus[half:], -1), 2, half)]
    else:
        pieces = [(b, 0, 0)] + [(shift(b, s), s, 0) for s in range(1, ny)]
    out = jnp.zeros((rows, 2 * ny * width), b.dtype)
    for mine, s, row in pieces:
        other = lax.ppermute(mine, "core", swap)
        chip = (y + s) % ny
        out = lax.dynamic_update_slice(out, mine, (row, (2 * chip + core) * width))
        out = lax.dynamic_update_slice(out, other, (row, (2 * chip + 1 - core) * width))
    return out


def make_shards(nz, nx, ny, ncore):
    def shards(gradients, weights, first_moment, second_moment):
        local_grad = gradients[0]
        row_count = weights.shape[0]
        seg_table = group_table(row_count)
        total, own = dp_sum(local_grad, nz, nx)
        grad = total / (nz * nx)
        part = own.shape[0]
        start = lax.axis_index("x") * part

        def rows_of(a):
            return lax.dynamic_slice_in_dim(a, start, part, 0)

        _, _, own_update = adam_part(
            own / (nz * nx), rows_of(weights), rows_of(first_moment), rows_of(second_moment), rows_of(seg_table)
        )
        both = jnp.concatenate([group_squares(weights, seg_table), group_squares(own_update, rows_of(seg_table))])
        both = tensor_sum(both, ny, ncore)
        weight_total, step_total = both[:4], axis_sum(both[4:], "x", nx)
        first_new, second_new, update = adam_part(grad, weights, first_moment, second_moment, seg_table)
        weights_new, ratios = apply_ratios(weights, update, seg_table, weight_total, step_total)
        if ncore == 2:
            copies = tensor_gather(weights_new.astype(jnp.bfloat16), ny)
        else:
            copies = lax.all_gather(weights_new.astype(jnp.bfloat16), TN, axis=1, tiled=True)
        return (weights_new, first_new, second_new, copies, ratios)

    return shards


def physical_mesh(mesh):
    devices = mesh.devices
    dp_devices = devices[:, 0]
    nx = len({d.coords[0] for d in dp_devices})
    nz = dp_devices.size // nx
    tn_devices = devices[0, :]
    ncore = len({d.core_on_chip for d in tn_devices})
    ny = tn_devices.size // ncore
    return Mesh(devices.reshape(nz, nx, ny, ncore), ("z", "x", "y", "core")), (nz, nx, ny, ncore)


def solution(mesh):
    mesh2, sizes = physical_mesh(mesh)
    return jax.shard_map(
        make_shards(*sizes),
        mesh=mesh2,
        in_specs=(P(DP, None, TN), P(None, TN), P(None, TN), P(None, TN)),
        out_specs=(P(None, TN), P(None, TN), P(None, TN), P(), P()),
        check_vma=False,
    )
```

```python
import jax
import jax.numpy as jnp
import numpy as np
from jax import lax
from jax.sharding import Mesh
from jax.sharding import PartitionSpec as P

D = 1024
HID = 1342


beta_one = 0.9
beta_two = 0.999
correct_one = 1.0 - 0.9**20
correct_two = 1.0 - 0.999**20
epsilon = 1e-06
learn_rate = 0.01
decay_rate = 0.01

DP = ("zh", "zl", "x")
TN = ("y", "core")


def group_table(row_count):
    row_ids = lax.broadcasted_iota(jnp.int32, (row_count, 4), 0)
    which = lax.broadcasted_iota(jnp.int32, (row_count, 4), 1)
    group = jnp.where(row_ids < D, 0, jnp.where(row_ids < D + HID, 1, row_ids - D - HID + 2))
    return (group == which).astype(jnp.float32)


def group_squares(values, seg_table):
    row_sums = jnp.sum(values * values, axis=1)
    return jnp.dot(row_sums, seg_table, precision=lax.Precision.HIGHEST)


def adam_part(grad, weights, first_moment, second_moment, seg_table):
    first_new = beta_one * first_moment + (1.0 - beta_one) * grad
    second_new = beta_two * second_moment + (1.0 - beta_two) * grad * grad
    decay = decay_rate * (seg_table[:, 0] + seg_table[:, 1])
    update = (
        first_new / correct_one / (jnp.sqrt(second_new / correct_two) + epsilon)
        + decay[:, None] * weights
    )
    return (first_new, second_new, update)


def apply_ratios(weights, update, seg_table, weight_total, step_total):
    ratios = jnp.sqrt(weight_total) / jnp.sqrt(step_total)
    row_ratio = jnp.dot(seg_table, ratios, precision=lax.Precision.HIGHEST)
    return (weights - learn_rate * row_ratio[:, None] * update, ratios)


def dp_sum(x, nz, nx):
    rows, cols = x.shape
    part = rows // nx
    padded = -(-part // (16 * nz)) * (16 * nz)
    half = padded // 2
    y = lax.all_to_all(x.reshape(nx, part, cols), "x", 0, 0, tiled=False).sum(0)
    y = jnp.pad(y, ((0, padded - part), (0, 0)))
    zl = lax.axis_index("zl")
    swap = [(0, 1), (1, 0)]
    keep = lax.dynamic_slice_in_dim(y, zl * half, half, 0)
    send = lax.dynamic_slice_in_dim(y, (1 - zl) * half, half, 0)
    y = keep + lax.ppermute(send, "zl", swap)
    nh = nz // 2
    y = lax.all_to_all(y.reshape(nh, half // nh, cols), "zh", 0, 0, tiled=False).sum(0)
    y = lax.all_to_all(jnp.broadcast_to(y[None], (nh,) + y.shape), "zh", 0, 0, tiled=False)
    y = y.reshape(half, cols)
    got = lax.ppermute(y, "zl", swap)
    y = jnp.where(zl == 0, jnp.concatenate([y, got], 0), jnp.concatenate([got, y], 0))[:part]
    y = lax.all_to_all(jnp.broadcast_to(y[None], (nx,) + y.shape), "x", 0, 0, tiled=False)
    return y.reshape(rows, cols)


def tensor_sum(v, ny, ncore):
    if ncore == 2:
        v = v + lax.ppermute(v, "core", [(0, 1), (1, 0)])
    else:
        v = lax.psum(v, "core")
    y = lax.axis_index("y")
    slots = jnp.zeros((ny,) + v.shape, v.dtype)
    slots = lax.dynamic_update_index_in_dim(slots, v, y, 0)
    for s in range(1, ny):
        got = lax.ppermute(v, "y", [(i, (i - s) % ny) for i in range(ny)])
        slots = lax.dynamic_update_index_in_dim(slots, got, (y + s) % ny, 0)
    total = slots[0]
    for k in range(1, ny):
        total = total + slots[k]
    return total


def tensor_gather(b, ny):
    y = lax.axis_index("y")
    core = lax.axis_index("core")
    swap = [(0, 1), (1, 0)]
    rows, width = b.shape

    def shift(v, s):
        return lax.ppermute(v, "y", [(i, (i - s) % ny) for i in range(ny)])

    if ny == 4 and rows % 16 == 0:
        half = rows // 2
        plus, minus = shift(b, 1), shift(b, -1)
        pieces = [(b, 0, 0), (plus, 1, 0), (minus, 3, 0), (shift(plus[:half], 1), 2, 0), (shift(minus[half:], -1), 2, half)]
    else:
        pieces = [(b, 0, 0)] + [(shift(b, s), s, 0) for s in range(1, ny)]
    out = jnp.zeros((rows, 2 * ny * width), b.dtype)
    for mine, s, row in pieces:
        other = lax.ppermute(mine, "core", swap)
        chip = (y + s) % ny
        out = lax.dynamic_update_slice(out, mine, (row, (2 * chip + core) * width))
        out = lax.dynamic_update_slice(out, other, (row, (2 * chip + 1 - core) * width))
    return out


def make_shards(nz, nx, ny, ncore):
    def shards(gradients, weights, first_moment, second_moment):
        local_grad = gradients[0]
        row_count = weights.shape[0]
        seg_table = group_table(row_count)
        grad = dp_sum(local_grad, nz, nx) / (nz * nx)
        first_new, second_new, update = adam_part(grad, weights, first_moment, second_moment, seg_table)
        both = jnp.concatenate([group_squares(weights, seg_table), group_squares(update, seg_table)])
        both = tensor_sum(both, ny, ncore)
        weight_total, step_total = both[:4], both[4:]
        weights_new, ratios = apply_ratios(weights, update, seg_table, weight_total, step_total)
        if ncore == 2:
            copies = tensor_gather(weights_new.astype(jnp.bfloat16), ny)
        else:
            copies = lax.all_gather(weights_new.astype(jnp.bfloat16), TN, axis=1, tiled=True)
        return (weights_new, first_new, second_new, copies, ratios)

    return shards


def physical_mesh(mesh):
    devices = mesh.devices
    dp_devices = devices[:, 0]
    nx = len({d.coords[0] for d in dp_devices})
    nz = dp_devices.size // nx
    tn_devices = devices[0, :]
    ncore = len({d.core_on_chip for d in tn_devices})
    ny = tn_devices.size // ncore
    return Mesh(devices.reshape(nz // 2, 2, nx, ny, ncore), ("zh", "zl", "x", "y", "core")), (nz, nx, ny, ncore)


def solution(mesh):
    mesh2, sizes = physical_mesh(mesh)
    return jax.shard_map(
        make_shards(*sizes),
        mesh=mesh2,
        in_specs=(P(DP, None, TN), P(None, TN), P(None, TN), P(None, TN)),
        out_specs=(P(None, TN), P(None, TN), P(None, TN), P(), P()),
        check_vma=False,
    )
```

```python
import jax
import jax.numpy as jnp
import numpy as np
from jax import lax
from jax.sharding import Mesh
from jax.sharding import PartitionSpec as P

D = 1024
HID = 1342


beta_one = 0.9
beta_two = 0.999
correct_one = 1.0 - 0.9**20
correct_two = 1.0 - 0.999**20
epsilon = 1e-06
learn_rate = 0.01
decay_rate = 0.01

DP = ("z", "x")
TN = ("y", "core")


def group_table(row_count):
    row_ids = lax.broadcasted_iota(jnp.int32, (row_count, 4), 0)
    which = lax.broadcasted_iota(jnp.int32, (row_count, 4), 1)
    group = jnp.where(row_ids < D, 0, jnp.where(row_ids < D + HID, 1, row_ids - D - HID + 2))
    return (group == which).astype(jnp.float32)


def group_squares(values, seg_table):
    row_sums = jnp.sum(values * values, axis=1)
    return jnp.dot(row_sums, seg_table, precision=lax.Precision.HIGHEST)


def adam_part(grad, weights, first_moment, second_moment, seg_table):
    first_new = beta_one * first_moment + (1.0 - beta_one) * grad
    second_new = beta_two * second_moment + (1.0 - beta_two) * grad * grad
    decay = decay_rate * (seg_table[:, 0] + seg_table[:, 1])
    update = (
        first_new / correct_one / (jnp.sqrt(second_new / correct_two) + epsilon)
        + decay[:, None] * weights
    )
    return (first_new, second_new, update)


def apply_ratios(weights, update, seg_table, weight_total, step_total):
    ratios = jnp.sqrt(weight_total) / jnp.sqrt(step_total)
    row_ratio = jnp.dot(seg_table, ratios, precision=lax.Precision.HIGHEST)
    return (weights - learn_rate * row_ratio[:, None] * update, ratios)


def dp_sum(x, nz, nx):
    rows, cols = x.shape
    part = rows // nx
    padded = -(-part // (8 * nz)) * (8 * nz)
    y = lax.all_to_all(x.reshape(nx, part, cols), "x", 0, 0, tiled=False).sum(0)
    y = jnp.pad(y, ((0, padded - part), (0, 0)))
    y = lax.all_to_all(y.reshape(nz, padded // nz, cols), "z", 0, 0, tiled=False).sum(0)
    y = lax.all_to_all(jnp.broadcast_to(y[None], (nz,) + y.shape), "z", 0, 0, tiled=False)
    y = y.reshape(padded, cols)[:part]
    if nx == 4 and part % 16 == 0:
        return ring_gather_rows(y, "x", nx)
    y = lax.all_to_all(jnp.broadcast_to(y[None], (nx,) + y.shape), "x", 0, 0, tiled=False)
    return y.reshape(rows, cols)


def ring_gather_rows(v, axis, n):
    me = lax.axis_index(axis)
    rows = v.shape[0]
    half = rows // 2

    def shift(a, s):
        return lax.ppermute(a, axis, [(i, (i - s) % n) for i in range(n)])

    plus, minus = shift(v, 1), shift(v, -1)
    pieces = [(v, 0, 0), (plus, 1, 0), (minus, n - 1, 0), (shift(plus[:half], 1), 2, 0), (shift(minus[half:], -1), 2, half)]
    out = jnp.zeros((n * rows,) + v.shape[1:], v.dtype)
    for piece, s, row in pieces:
        out = lax.dynamic_update_slice_in_dim(out, piece, ((me + s) % n) * rows + row, 0)
    return out


def tensor_sum(v, ny, ncore):
    if ncore == 2:
        v = v + lax.ppermute(v, "core", [(0, 1), (1, 0)])
    else:
        v = lax.psum(v, "core")
    y = lax.axis_index("y")
    slots = jnp.zeros((ny,) + v.shape, v.dtype)
    slots = lax.dynamic_update_index_in_dim(slots, v, y, 0)
    for s in range(1, ny):
        got = lax.ppermute(v, "y", [(i, (i - s) % ny) for i in range(ny)])
        slots = lax.dynamic_update_index_in_dim(slots, got, (y + s) % ny, 0)
    total = slots[0]
    for k in range(1, ny):
        total = total + slots[k]
    return total


def tensor_gather(b, ny):
    y = lax.axis_index("y")
    core = lax.axis_index("core")
    swap = [(0, 1), (1, 0)]
    rows, width = b.shape

    def shift(v, s):
        return lax.ppermute(v, "y", [(i, (i - s) % ny) for i in range(ny)])

    if ny == 4 and rows % 16 == 0:
        half = rows // 2
        plus, minus = shift(b, 1), shift(b, -1)
        pieces = [(b, 0, 0), (plus, 1, 0), (minus, 3, 0), (shift(plus[:half], 1), 2, 0), (shift(minus[half:], -1), 2, half)]
    else:
        pieces = [(b, 0, 0)] + [(shift(b, s), s, 0) for s in range(1, ny)]
    out = jnp.zeros((rows, 2 * ny * width), b.dtype)
    for mine, s, row in pieces:
        other = lax.ppermute(mine, "core", swap)
        chip = (y + s) % ny
        out = lax.dynamic_update_slice(out, mine, (row, (2 * chip + core) * width))
        out = lax.dynamic_update_slice(out, other, (row, (2 * chip + 1 - core) * width))
    return out


def make_shards(nz, nx, ny, ncore):
    def shards(gradients, weights, first_moment, second_moment):
        local_grad = gradients[0]
        row_count = weights.shape[0]
        seg_table = group_table(row_count)
        grad = dp_sum(local_grad, nz, nx) / (nz * nx)
        first_new, second_new, update = adam_part(grad, weights, first_moment, second_moment, seg_table)
        both = jnp.concatenate([group_squares(weights, seg_table), group_squares(update, seg_table)])
        both = tensor_sum(both, ny, ncore)
        weight_total, step_total = both[:4], both[4:]
        weights_new, ratios = apply_ratios(weights, update, seg_table, weight_total, step_total)
        if ncore == 2:
            copies = tensor_gather(weights_new.astype(jnp.bfloat16), ny)
        else:
            copies = lax.all_gather(weights_new.astype(jnp.bfloat16), TN, axis=1, tiled=True)
        return (weights_new, first_new, second_new, copies, ratios)

    return shards


def physical_mesh(mesh):
    devices = mesh.devices
    dp_devices = devices[:, 0]
    nx = len({d.coords[0] for d in dp_devices})
    nz = dp_devices.size // nx
    tn_devices = devices[0, :]
    ncore = len({d.core_on_chip for d in tn_devices})
    ny = tn_devices.size // ncore
    return Mesh(devices.reshape(nz, nx, ny, ncore), ("z", "x", "y", "core")), (nz, nx, ny, ncore)


def solution(mesh):
    mesh2, sizes = physical_mesh(mesh)
    return jax.shard_map(
        make_shards(*sizes),
        mesh=mesh2,
        in_specs=(P(DP, None, TN), P(None, TN), P(None, TN), P(None, TN)),
        out_specs=(P(None, TN), P(None, TN), P(None, TN), P(), P()),
        check_vma=False,
    )
```

```python
import jax
import jax.numpy as jnp
import numpy as np
from jax import lax
from jax.sharding import Mesh
from jax.sharding import PartitionSpec as P

D = 1024
HID = 1342


beta_one = 0.9
beta_two = 0.999
correct_one = 1.0 - 0.9**20
correct_two = 1.0 - 0.999**20
epsilon = 1e-06
learn_rate = 0.01
decay_rate = 0.01

DP = ("z", "x")
TN = ("y", "core")


def group_table(row_count):
    row_ids = lax.broadcasted_iota(jnp.int32, (row_count, 4), 0)
    which = lax.broadcasted_iota(jnp.int32, (row_count, 4), 1)
    group = jnp.where(row_ids < D, 0, jnp.where(row_ids < D + HID, 1, row_ids - D - HID + 2))
    return (group == which).astype(jnp.float32)


def group_squares(values, seg_table):
    row_sums = jnp.sum(values * values, axis=1)
    return jnp.dot(row_sums, seg_table, precision=lax.Precision.HIGHEST)


def adam_part(grad, weights, first_moment, second_moment, seg_table):
    first_new = beta_one * first_moment + (1.0 - beta_one) * grad
    second_new = beta_two * second_moment + (1.0 - beta_two) * grad * grad
    decay = decay_rate * (seg_table[:, 0] + seg_table[:, 1])
    update = (
        first_new / correct_one / (jnp.sqrt(second_new / correct_two) + epsilon)
        + decay[:, None] * weights
    )
    return (first_new, second_new, update)


def apply_ratios(weights, update, seg_table, weight_total, step_total):
    ratios = jnp.sqrt(weight_total) / jnp.sqrt(step_total)
    row_ratio = jnp.dot(seg_table, ratios, precision=lax.Precision.HIGHEST)
    return (weights - learn_rate * row_ratio[:, None] * update, ratios)


def dp_sum(x, nz, nx):
    rows, cols = x.shape
    part = rows // nx
    padded = -(-part // (8 * nz)) * (8 * nz)
    y = lax.all_to_all(x.reshape(nx, part, cols), "x", 0, 0, tiled=False).sum(0)
    y = jnp.pad(y, ((0, padded - part), (0, 0)))
    y = lax.all_to_all(y.reshape(nz, padded // nz, cols), "z", 0, 0, tiled=False).sum(0)
    y = lax.all_to_all(jnp.broadcast_to(y[None], (nz,) + y.shape), "z", 0, 0, tiled=False)
    y = y.reshape(padded, cols)[:part]
    y = lax.all_to_all(jnp.broadcast_to(y[None], (nx,) + y.shape), "x", 0, 0, tiled=False)
    return y.reshape(rows, cols)


def tensor_sum(v, ny, ncore):
    if ncore == 2:
        v = v + lax.ppermute(v, "core", [(0, 1), (1, 0)])
    else:
        v = lax.psum(v, "core")
    y = lax.axis_index("y")
    slots = jnp.zeros((ny,) + v.shape, v.dtype)
    slots = lax.dynamic_update_index_in_dim(slots, v, y, 0)
    for s in range(1, ny):
        got = lax.ppermute(v, "y", [(i, (i - s) % ny) for i in range(ny)])
        slots = lax.dynamic_update_index_in_dim(slots, got, (y + s) % ny, 0)
    total = slots[0]
    for k in range(1, ny):
        total = total + slots[k]
    return total


def tensor_gather(b, ny):
    y = lax.axis_index("y")
    core = lax.axis_index("core")
    swap = [(0, 1), (1, 0)]
    rows, width = b.shape

    def shift(v, s):
        return lax.ppermute(v, "y", [(i, (i - s) % ny) for i in range(ny)])

    if ny == 4 and rows % 16 == 0:
        half = rows // 2
        plus, minus = shift(b, 1), shift(b, -1)
        pieces = [(b, 0, 0), (plus, 1, 0), (minus, 3, 0), (shift(plus[:half], 1), 2, 0), (shift(minus[half:], -1), 2, half)]
    else:
        pieces = [(b, 0, 0)] + [(shift(b, s), s, 0) for s in range(1, ny)]
    first = pieces[1][0]
    out = jnp.tile(first, (1, 2 * ny))
    for mine, s, row in pieces:
        other = lax.ppermute(mine, "core", swap)
        chip = (y + s) % ny
        out = lax.dynamic_update_slice(out, mine, (row, (2 * chip + core) * width))
        out = lax.dynamic_update_slice(out, other, (row, (2 * chip + 1 - core) * width))
    return out


def make_shards(nz, nx, ny, ncore):
    def shards(gradients, weights, first_moment, second_moment):
        local_grad = gradients[0]
        row_count = weights.shape[0]
        seg_table = group_table(row_count)
        grad = dp_sum(local_grad, nz, nx) / (nz * nx)
        first_new, second_new, update = adam_part(grad, weights, first_moment, second_moment, seg_table)
        both = jnp.concatenate([group_squares(weights, seg_table), group_squares(update, seg_table)])
        both = tensor_sum(both, ny, ncore)
        weight_total, step_total = both[:4], both[4:]
        weights_new, ratios = apply_ratios(weights, update, seg_table, weight_total, step_total)
        if ncore == 2:
            copies = tensor_gather(weights_new.astype(jnp.bfloat16), ny)
        else:
            copies = lax.all_gather(weights_new.astype(jnp.bfloat16), TN, axis=1, tiled=True)
        return (weights_new, first_new, second_new, copies, ratios)

    return shards


def physical_mesh(mesh):
    devices = mesh.devices
    dp_devices = devices[:, 0]
    nx = len({d.coords[0] for d in dp_devices})
    nz = dp_devices.size // nx
    tn_devices = devices[0, :]
    ncore = len({d.core_on_chip for d in tn_devices})
    ny = tn_devices.size // ncore
    return Mesh(devices.reshape(nz, nx, ny, ncore), ("z", "x", "y", "core")), (nz, nx, ny, ncore)


def solution(mesh):
    mesh2, sizes = physical_mesh(mesh)
    return jax.shard_map(
        make_shards(*sizes),
        mesh=mesh2,
        in_specs=(P(DP, None, TN), P(None, TN), P(None, TN), P(None, TN)),
        out_specs=(P(None, TN), P(None, TN), P(None, TN), P(), P()),
        check_vma=False,
    )
```

```python
import jax
import jax.numpy as jnp
import numpy as np
from jax import lax
from jax.sharding import Mesh
from jax.sharding import PartitionSpec as P

D = 1024
HID = 1342


beta_one = 0.9
beta_two = 0.999
correct_one = 1.0 - 0.9**20
correct_two = 1.0 - 0.999**20
epsilon = 1e-06
learn_rate = 0.01
decay_rate = 0.01

DP = ("z", "x")
TN = ("y", "core")


def group_table(row_count):
    row_ids = lax.broadcasted_iota(jnp.int32, (row_count, 4), 0)
    which = lax.broadcasted_iota(jnp.int32, (row_count, 4), 1)
    group = jnp.where(row_ids < D, 0, jnp.where(row_ids < D + HID, 1, row_ids - D - HID + 2))
    return (group == which).astype(jnp.float32)


def group_squares(values, seg_table):
    row_sums = jnp.sum(values * values, axis=1)
    return jnp.dot(row_sums, seg_table, precision=lax.Precision.HIGHEST)


def adam_part(grad, weights, first_moment, second_moment, seg_table):
    first_new = beta_one * first_moment + (1.0 - beta_one) * grad
    second_new = beta_two * second_moment + (1.0 - beta_two) * grad * grad
    decay = decay_rate * (seg_table[:, 0] + seg_table[:, 1])
    update = (
        first_new / correct_one / (jnp.sqrt(second_new / correct_two) + epsilon)
        + decay[:, None] * weights
    )
    return (first_new, second_new, update)


def apply_ratios(weights, update, seg_table, weight_total, step_total):
    ratios = jnp.sqrt(weight_total) / jnp.sqrt(step_total)
    row_ratio = jnp.dot(seg_table, ratios, precision=lax.Precision.HIGHEST)
    return (weights - learn_rate * row_ratio[:, None] * update, ratios)


def dp_sum(x, nz, nx):
    rows, cols = x.shape
    part = rows // nx
    padded = -(-part // (8 * nz)) * (8 * nz)
    y = lax.all_to_all(x.reshape(nx, part, cols), "x", 0, 0, tiled=False).sum(0)
    y = jnp.pad(y, ((0, padded - part), (0, 0)))
    y = lax.all_to_all(y.reshape(nz, padded // nz, cols), "z", 0, 0, tiled=False).sum(0)
    y = lax.all_to_all(jnp.broadcast_to(y[None], (nz,) + y.shape), "z", 0, 0, tiled=False)
    y = y.reshape(padded, cols)[:part]
    y = lax.all_to_all(jnp.broadcast_to(y[None], (nx,) + y.shape), "x", 0, 0, tiled=False)
    return y.reshape(rows, cols)


def tensor_sum(v, ny, ncore):
    if ncore == 2:
        v = v + lax.ppermute(v, "core", [(0, 1), (1, 0)])
    else:
        v = lax.psum(v, "core")
    y = lax.axis_index("y")
    slots = jnp.zeros((ny,) + v.shape, v.dtype)
    slots = lax.dynamic_update_index_in_dim(slots, v, y, 0)
    for s in range(1, ny):
        got = lax.ppermute(v, "y", [(i, (i - s) % ny) for i in range(ny)])
        slots = lax.dynamic_update_index_in_dim(slots, got, (y + s) % ny, 0)
    total = slots[0]
    for k in range(1, ny):
        total = total + slots[k]
    return total


def tensor_gather(b, ny):
    y = lax.axis_index("y")
    core = lax.axis_index("core")
    swap = [(0, 1), (1, 0)]
    rows, width = b.shape

    def shift(v, s):
        return lax.ppermute(v, "y", [(i, (i - s) % ny) for i in range(ny)])

    if ny == 4 and rows % 16 == 0:
        half = rows // 2
        plus, minus = shift(b, 1), shift(b, -1)
        pieces = [(b, 0, 0), (plus, 1, 0), (minus, 3, 0), (shift(plus[:half], 1), 2, 0), (shift(minus[half:], -1), 2, half)]
    else:
        pieces = [(b, 0, 0)] + [(shift(b, s), s, 0) for s in range(1, ny)]
    others = [lax.ppermute(mine, "core", swap) for mine, _, _ in pieces]
    out = jnp.tile(others[0], (1, 2 * ny))
    for (mine, s, row), other in zip(pieces, others):
        chip = (y + s) % ny
        out = lax.dynamic_update_slice(out, mine, (row, (2 * chip + core) * width))
        out = lax.dynamic_update_slice(out, other, (row, (2 * chip + 1 - core) * width))
    return out


def make_shards(nz, nx, ny, ncore):
    def shards(gradients, weights, first_moment, second_moment):
        local_grad = gradients[0]
        row_count = weights.shape[0]
        seg_table = group_table(row_count)
        grad = dp_sum(local_grad, nz, nx) / (nz * nx)
        first_new, second_new, update = adam_part(grad, weights, first_moment, second_moment, seg_table)
        both = jnp.concatenate([group_squares(weights, seg_table), group_squares(update, seg_table)])
        both = tensor_sum(both, ny, ncore)
        weight_total, step_total = both[:4], both[4:]
        weights_new, ratios = apply_ratios(weights, update, seg_table, weight_total, step_total)
        if ncore == 2:
            copies = tensor_gather(weights_new.astype(jnp.bfloat16), ny)
        else:
            copies = lax.all_gather(weights_new.astype(jnp.bfloat16), TN, axis=1, tiled=True)
        return (weights_new, first_new, second_new, copies, ratios)

    return shards


def physical_mesh(mesh):
    devices = mesh.devices
    dp_devices = devices[:, 0]
    nx = len({d.coords[0] for d in dp_devices})
    nz = dp_devices.size // nx
    tn_devices = devices[0, :]
    ncore = len({d.core_on_chip for d in tn_devices})
    ny = tn_devices.size // ncore
    return Mesh(devices.reshape(nz, nx, ny, ncore), ("z", "x", "y", "core")), (nz, nx, ny, ncore)


def solution(mesh):
    mesh2, sizes = physical_mesh(mesh)
    return jax.shard_map(
        make_shards(*sizes),
        mesh=mesh2,
        in_specs=(P(DP, None, TN), P(None, TN), P(None, TN), P(None, TN)),
        out_specs=(P(None, TN), P(None, TN), P(None, TN), P(), P()),
        check_vma=False,
    )
```

```python
import jax
import jax.numpy as jnp
import numpy as np
from jax import lax
from jax.sharding import Mesh
from jax.sharding import PartitionSpec as P

D = 1024
HID = 1342


beta_one = 0.9
beta_two = 0.999
correct_one = 1.0 - 0.9**20
correct_two = 1.0 - 0.999**20
epsilon = 1e-06
learn_rate = 0.01
decay_rate = 0.01

DP = ("z", "x")
TN = ("y", "core")


def group_table(row_count):
    row_ids = lax.broadcasted_iota(jnp.int32, (row_count, 4), 0)
    which = lax.broadcasted_iota(jnp.int32, (row_count, 4), 1)
    group = jnp.where(row_ids < D, 0, jnp.where(row_ids < D + HID, 1, row_ids - D - HID + 2))
    return (group == which).astype(jnp.float32)


def group_squares(values, seg_table):
    row_sums = jnp.sum(values * values, axis=1)
    return jnp.dot(row_sums, seg_table, precision=lax.Precision.HIGHEST)


def adam_part(grad, weights, first_moment, second_moment, seg_table):
    first_new = beta_one * first_moment + (1.0 - beta_one) * grad
    second_new = beta_two * second_moment + (1.0 - beta_two) * grad * grad
    decay = decay_rate * (seg_table[:, 0] + seg_table[:, 1])
    update = (
        first_new / correct_one / (jnp.sqrt(second_new / correct_two) + epsilon)
        + decay[:, None] * weights
    )
    return (first_new, second_new, update)


def apply_ratios(weights, update, seg_table, weight_total, step_total):
    ratios = jnp.sqrt(weight_total) / jnp.sqrt(step_total)
    row_ratio = jnp.dot(seg_table, ratios, precision=lax.Precision.HIGHEST)
    return (weights - learn_rate * row_ratio[:, None] * update, ratios)


def dp_sum(x, nz, nx):
    rows, cols = x.shape
    part = rows // nx
    padded = -(-part // (8 * nz)) * (8 * nz)
    y = lax.all_to_all(x.reshape(nx, part, cols), "x", 0, 0, tiled=False).sum(0)
    y = jnp.pad(y, ((0, padded - part), (0, 0)))
    y = lax.all_to_all(y.reshape(nz, padded // nz, cols), "z", 0, 0, tiled=False).sum(0)
    y = lax.all_to_all(jnp.broadcast_to(y[None], (nz,) + y.shape), "z", 0, 0, tiled=False)
    y = y.reshape(padded, cols)[:part]
    y = lax.all_to_all(jnp.broadcast_to(y[None], (nx,) + y.shape), "x", 0, 0, tiled=False)
    return y.reshape(rows, cols)


def tensor_sum(v, ny, ncore):
    n = ny * ncore
    me = lax.axis_index(TN)
    slots = jnp.zeros((n,) + v.shape, v.dtype)
    slots = lax.dynamic_update_index_in_dim(slots, v, me, 0)
    for s in range(1, n):
        got = lax.ppermute(v, TN, [(i, (i - s) % n) for i in range(n)])
        slots = lax.dynamic_update_index_in_dim(slots, got, (me + s) % n, 0)
    total = slots[0]
    for k in range(1, n):
        total = total + slots[k]
    return total


def tensor_gather(b, ny):
    y = lax.axis_index("y")
    core = lax.axis_index("core")
    swap = [(0, 1), (1, 0)]
    rows, width = b.shape

    def shift(v, s):
        return lax.ppermute(v, "y", [(i, (i - s) % ny) for i in range(ny)])

    if ny == 4 and rows % 16 == 0:
        half = rows // 2
        plus, minus = shift(b, 1), shift(b, -1)
        pieces = [(b, 0, 0), (plus, 1, 0), (minus, 3, 0), (shift(plus[:half], 1), 2, 0), (shift(minus[half:], -1), 2, half)]
    else:
        pieces = [(b, 0, 0)] + [(shift(b, s), s, 0) for s in range(1, ny)]
    others = [lax.ppermute(mine, "core", swap) for mine, _, _ in pieces]
    out = jnp.tile(others[0], (1, 2 * ny))
    for (mine, s, row), other in zip(pieces, others):
        chip = (y + s) % ny
        out = lax.dynamic_update_slice(out, mine, (row, (2 * chip + core) * width))
        out = lax.dynamic_update_slice(out, other, (row, (2 * chip + 1 - core) * width))
    return out


def make_shards(nz, nx, ny, ncore):
    def shards(gradients, weights, first_moment, second_moment):
        local_grad = gradients[0]
        row_count = weights.shape[0]
        seg_table = group_table(row_count)
        grad = dp_sum(local_grad, nz, nx) / (nz * nx)
        first_new, second_new, update = adam_part(grad, weights, first_moment, second_moment, seg_table)
        both = jnp.concatenate([group_squares(weights, seg_table), group_squares(update, seg_table)])
        both = tensor_sum(both, ny, ncore)
        weight_total, step_total = both[:4], both[4:]
        weights_new, ratios = apply_ratios(weights, update, seg_table, weight_total, step_total)
        if ncore == 2:
            copies = tensor_gather(weights_new.astype(jnp.bfloat16), ny)
        else:
            copies = lax.all_gather(weights_new.astype(jnp.bfloat16), TN, axis=1, tiled=True)
        return (weights_new, first_new, second_new, copies, ratios)

    return shards


def physical_mesh(mesh):
    devices = mesh.devices
    dp_devices = devices[:, 0]
    nx = len({d.coords[0] for d in dp_devices})
    nz = dp_devices.size // nx
    tn_devices = devices[0, :]
    ncore = len({d.core_on_chip for d in tn_devices})
    ny = tn_devices.size // ncore
    return Mesh(devices.reshape(nz, nx, ny, ncore), ("z", "x", "y", "core")), (nz, nx, ny, ncore)


def solution(mesh):
    mesh2, sizes = physical_mesh(mesh)
    return jax.shard_map(
        make_shards(*sizes),
        mesh=mesh2,
        in_specs=(P(DP, None, TN), P(None, TN), P(None, TN), P(None, TN)),
        out_specs=(P(None, TN), P(None, TN), P(None, TN), P(), P()),
        check_vma=False,
    )
```

```python
import jax
import jax.numpy as jnp
import numpy as np
from jax import lax
from jax.sharding import Mesh
from jax.sharding import PartitionSpec as P

D = 1024
HID = 1342


beta_one = 0.9
beta_two = 0.999
correct_one = 1.0 - 0.9**20
correct_two = 1.0 - 0.999**20
epsilon = 1e-06
learn_rate = 0.01
decay_rate = 0.01

DP = ("z", "x")
TN = ("y", "core")


def group_table(row_count):
    row_ids = lax.broadcasted_iota(jnp.int32, (row_count, 4), 0)
    which = lax.broadcasted_iota(jnp.int32, (row_count, 4), 1)
    group = jnp.where(row_ids < D, 0, jnp.where(row_ids < D + HID, 1, row_ids - D - HID + 2))
    return (group == which).astype(jnp.float32)


def group_squares(values, seg_table):
    row_sums = jnp.sum(values * values, axis=1)
    return jnp.dot(row_sums, seg_table, precision=lax.Precision.HIGHEST)


def adam_part(grad, weights, first_moment, second_moment, seg_table):
    first_new = beta_one * first_moment + (1.0 - beta_one) * grad
    second_new = beta_two * second_moment + (1.0 - beta_two) * grad * grad
    decay = decay_rate * (seg_table[:, 0] + seg_table[:, 1])
    update = (
        first_new / correct_one / (jnp.sqrt(second_new / correct_two) + epsilon)
        + decay[:, None] * weights
    )
    return (first_new, second_new, update)


def apply_ratios(weights, update, seg_table, weight_total, step_total):
    ratios = jnp.sqrt(weight_total) / jnp.sqrt(step_total)
    row_ratio = jnp.dot(seg_table, ratios, precision=lax.Precision.HIGHEST)
    return (weights - learn_rate * row_ratio[:, None] * update, ratios)


def dp_sum(x, nz, nx):
    rows, cols = x.shape
    part = rows // nx
    padded = -(-part // (8 * nz)) * (8 * nz)
    y = lax.all_to_all(x.reshape(nx, part, cols), "x", 0, 0, tiled=False).sum(0)
    y = jnp.pad(y, ((0, padded - part), (0, 0)))
    y = lax.all_to_all(y.reshape(nz, padded // nz, cols), "z", 0, 0, tiled=False).sum(0)
    y = lax.all_to_all(jnp.broadcast_to(y[None], (nz,) + y.shape), "z", 0, 0, tiled=False)
    y = y.reshape(padded, cols)[:part]
    y = lax.all_to_all(jnp.broadcast_to(y[None], (nx,) + y.shape), "x", 0, 0, tiled=False)
    return y.reshape(rows, cols)


def tensor_sum(v, ny, ncore):
    if ncore == 2:
        v = v + lax.ppermute(v, "core", [(0, 1), (1, 0)])
    else:
        v = lax.psum(v, "core")
    y = lax.axis_index("y")
    slots = jnp.zeros((ny,) + v.shape, v.dtype)
    slots = lax.dynamic_update_index_in_dim(slots, v, y, 0)

    def shift(a, s):
        return lax.ppermute(a, "y", [(i, (i - s) % ny) for i in range(ny)])

    if ny == 4:
        plus = shift(v, 1)
        got = [(plus, 1), (shift(v, -1), 3), (shift(plus, 1), 2)]
    else:
        got = [(shift(v, s), s) for s in range(1, ny)]
    for value, s in got:
        slots = lax.dynamic_update_index_in_dim(slots, value, (y + s) % ny, 0)
    total = slots[0]
    for k in range(1, ny):
        total = total + slots[k]
    return total


def tensor_gather(b, ny):
    y = lax.axis_index("y")
    core = lax.axis_index("core")
    swap = [(0, 1), (1, 0)]
    rows, width = b.shape

    def shift(v, s):
        return lax.ppermute(v, "y", [(i, (i - s) % ny) for i in range(ny)])

    if ny == 4 and rows % 16 == 0:
        half = rows // 2
        plus, minus = shift(b, 1), shift(b, -1)
        pieces = [(b, 0, 0), (plus, 1, 0), (minus, 3, 0), (shift(plus[:half], 1), 2, 0), (shift(minus[half:], -1), 2, half)]
    else:
        pieces = [(b, 0, 0)] + [(shift(b, s), s, 0) for s in range(1, ny)]
    others = [lax.ppermute(mine, "core", swap) for mine, _, _ in pieces]
    out = jnp.tile(others[0], (1, 2 * ny))
    for (mine, s, row), other in zip(pieces, others):
        chip = (y + s) % ny
        out = lax.dynamic_update_slice(out, mine, (row, (2 * chip + core) * width))
        out = lax.dynamic_update_slice(out, other, (row, (2 * chip + 1 - core) * width))
    return out


def make_shards(nz, nx, ny, ncore):
    def shards(gradients, weights, first_moment, second_moment):
        local_grad = gradients[0]
        row_count = weights.shape[0]
        seg_table = group_table(row_count)
        grad = dp_sum(local_grad, nz, nx) / (nz * nx)
        first_new, second_new, update = adam_part(grad, weights, first_moment, second_moment, seg_table)
        both = jnp.concatenate([group_squares(weights, seg_table), group_squares(update, seg_table)])
        both = tensor_sum(both, ny, ncore)
        weight_total, step_total = both[:4], both[4:]
        weights_new, ratios = apply_ratios(weights, update, seg_table, weight_total, step_total)
        if ncore == 2:
            copies = tensor_gather(weights_new.astype(jnp.bfloat16), ny)
        else:
            copies = lax.all_gather(weights_new.astype(jnp.bfloat16), TN, axis=1, tiled=True)
        return (weights_new, first_new, second_new, copies, ratios)

    return shards


def physical_mesh(mesh):
    devices = mesh.devices
    dp_devices = devices[:, 0]
    nx = len({d.coords[0] for d in dp_devices})
    nz = dp_devices.size // nx
    tn_devices = devices[0, :]
    ncore = len({d.core_on_chip for d in tn_devices})
    ny = tn_devices.size // ncore
    return Mesh(devices.reshape(nz, nx, ny, ncore), ("z", "x", "y", "core")), (nz, nx, ny, ncore)


def solution(mesh):
    mesh2, sizes = physical_mesh(mesh)
    return jax.shard_map(
        make_shards(*sizes),
        mesh=mesh2,
        in_specs=(P(DP, None, TN), P(None, TN), P(None, TN), P(None, TN)),
        out_specs=(P(None, TN), P(None, TN), P(None, TN), P(), P()),
        check_vma=False,
    )
```
